256 devices in a mesh: node: 16 (over y, x_hi, core), tm: 16 (over z, x_lo).
Axes of the slice: x: 4 (x_hi: 2, x_lo: 2; x = x_hi * 2 + x_lo), y: 4, z: 8, core: 2. Of those that a mesh axis runs over, the one named last changes fastest.
Arguments:
- observed: bfloat16 [65536, 16384], P('node', 'tm'), may hold values from 0.5 to 32
- node_factor: bfloat16 [64, 65536], P(None, ('node', 'tm')), may hold values from 0.19921875 to 1
- time_factor: bfloat16 [64, 1024], P(None, 'tm'), may hold values from 0.19921875 to 1
- species_factor: bfloat16 [64, 16], replicated, may hold values from 0.19921875 to 1
Outputs:
- grad_node: float32 [64, 65536], P(None, ('node', 'tm'))
- grad_time: float32 [64, 1024], P(None, 'tm')
- grad_species: float32 [64, 16], replicated
The draws below stay inside these ranges and needn't reach their ends.
All inputs are finite; a program needn't handle non-finite values.
Results may differ from the reference program's by a relative error of at most 0.0017.
Values may be sent and summed in bfloat16 or wider, within the bound.
No kernel may reach another device: no remote copies, remote signals or barrier semaphores. Data moves between devices by JAX's collectives and lax.ppermute only.
A program may use at most 64 MiB of HBM per device.

```python
import math
import jax
import jax.numpy as jnp
from jax import lax

R = 64
S = 16
NODES = 65536
STEPS = 1024


def level_of(key, shape, pieces, low, high):
    def one(axis_at, shards_of):
        steps = jax.random.uniform(jax.random.fold_in(jax.random.fold_in(key, 6), axis_at), (shards_of,), jnp.float32, low / len(pieces), high / len(pieces))
        return jnp.repeat(jnp.exp(steps), shape[axis_at] // shards_of).reshape((-1,) + (1,) * (len(shape) - axis_at - 1))

    level = one(*pieces[0])
    for cut in pieces[1:]:
        level = level * one(*cut)
    return level


def setup_inputs(seed: int = 0) -> dict:
    streams_of = jax.random.split(jax.random.key(seed), 5)
    observed = jnp.clip(jnp.exp(math.log(32.0) - 4.158883 * jax.random.uniform(streams_of[0], (NODES, STEPS * S), jnp.float32) ** level_of(streams_of[0], (NODES, STEPS * S), ((0, 16), (1, 16)), -0.2, 0.2)), 0.5, 32.0).astype(jnp.bfloat16)
    node_factor = jnp.clip(jnp.exp(math.log(1.0) - 1.6133518 * jax.random.uniform(streams_of[1], (R, NODES), jnp.float32) ** level_of(streams_of[1], (R, NODES), ((1, 256),), -0.2, 0.2)), 0.19921875, 1.0).astype(jnp.bfloat16)
    time_factor = jnp.clip(jnp.exp(math.log(1.0) - 1.6133518 * jax.random.uniform(streams_of[2], (R, STEPS), jnp.float32) ** level_of(streams_of[2], (R, STEPS), ((1, 16),), -0.2, 0.2)), 0.19921875, 1.0).astype(jnp.bfloat16)
    species_factor = jnp.clip(jnp.exp(jax.random.uniform(streams_of[3], (R, S), jnp.float32, math.log(0.19921875), math.log(1.0))), 0.19921875, 1.0).astype(jnp.bfloat16)
    return dict(observed=observed, node_factor=node_factor, time_factor=time_factor, species_factor=species_factor)


def widen(values):
    return lax.optimization_barrier(values).astype(jnp.float32)

def reference(observed, node_factor, time_factor, species_factor):
    factor_rank = node_factor.shape[0]
    time_vals = time_factor.astype(jnp.float32)
    species_vals = species_factor.astype(jnp.float32)
    khatri = (time_vals[:, :, None] * species_vals[:, None, :]).reshape(factor_rank, STEPS * S).astype(jnp.bfloat16)
    khatri_wide = widen(khatri)
    block_rows = math.gcd(NODES, 4096)
    nblocks = NODES // block_rows
    observed_blocks = observed.reshape(nblocks, block_rows, STEPS * S)
    factor_blocks = node_factor.T.reshape(nblocks, block_rows, factor_rank)

    def absorb_block(contracted, block_pair):
        observed_rows, factor_block = block_pair
        factor_wide = factor_block.astype(jnp.float32)
        modelled = jnp.dot(factor_wide, khatri_wide, precision=lax.Precision.HIGHEST)
        derivative = ((modelled - observed_rows.astype(jnp.float32)) / (modelled * modelled)).astype(jnp.bfloat16)
        derivative_wide = widen(derivative)
        node_part = jnp.dot(derivative_wide, khatri_wide.T, precision=lax.Precision.HIGHEST)
        contracted = contracted + jnp.dot(derivative_wide.T, factor_wide, precision=lax.Precision.HIGHEST)
        return (contracted, node_part)
    start_sum = jnp.zeros((STEPS * S, factor_rank), jnp.float32)
    contracted, node_parts = lax.scan(absorb_block, start_sum, (observed_blocks, factor_blocks))
    grad_node = node_parts.reshape(NODES, factor_rank).T / math.sqrt(STEPS * S)
    by_step = contracted.reshape(STEPS, S, factor_rank)
    grad_time = jnp.einsum('tsr,rs->rt', by_step, species_vals, precision=lax.Precision.HIGHEST) / math.sqrt(NODES * S)
    grad_species = jnp.einsum('tsr,rt->rs', by_step, time_vals, precision=lax.Precision.HIGHEST) / math.sqrt(NODES * STEPS)
    return (grad_node, grad_time, grad_species)
```

```python
import math

import jax
import jax.numpy as jnp
from jax import lax
from jax.sharding import PartitionSpec as P


def gather_blocks(values, axis):
    count = lax.axis_size(axis)
    copies = jnp.broadcast_to(values[None], (count, *values.shape))
    return lax.all_to_all(copies, axis, 0, 0, tiled=True)


def shards(observed, node_factor, time_factor, species_factor):
    factor_rank = node_factor.shape[0]
    time_vals = time_factor.astype(jnp.float32)
    species_vals = species_factor.astype(jnp.float32)
    time_dev = time_vals.shape[1]
    species = species_vals.shape[1]
    node_rows = observed.shape[0]
    flat_width = observed.shape[1]
    tm_count = lax.axis_size("tm")
    steps_all = time_dev * tm_count
    nodes_all = node_rows * lax.axis_size("node")
    share_rows = node_rows // tm_count

    khatri = (
        (time_vals[:, :, None] * species_vals[:, None, :])
        .reshape(factor_rank, flat_width)
        .astype(jnp.bfloat16)
    )
    gathered = gather_blocks(node_factor, "tm")
    factor = gathered.transpose(1, 0, 2).reshape(factor_rank, node_rows)
    modelled = lax.dot_general(
        factor, khatri, (((0,), (0,)), ((), ())), preferred_element_type=jnp.float32
    )
    derivative = ((modelled - observed.astype(jnp.float32)) / (modelled * modelled)).astype(
        jnp.bfloat16
    )
    node_part = lax.dot_general(
        khatri, derivative, (((1,), (1,)), ((), ())), preferred_element_type=jnp.float32
    )
    contracted = lax.dot_general(
        derivative, factor, (((0,), (1,)), ((), ())), preferred_element_type=jnp.float32
    )
    by_step = contracted.reshape(time_dev, species, factor_rank)
    time_part = jnp.einsum("tsr,rs->rt", by_step, species_vals, precision=lax.Precision.HIGHEST)
    species_part = jnp.einsum("tsr,rt->rs", by_step, time_vals, precision=lax.Precision.HIGHEST)

    blocks = node_part.reshape(factor_rank, tm_count, share_rows).transpose(1, 0, 2)
    riders = jnp.broadcast_to(species_part[None], (tm_count, factor_rank, species))
    payload = jnp.concatenate([blocks, riders], axis=2)
    summed = lax.all_to_all(payload, "tm", 0, 0, tiled=True).sum(0)
    grad_node = summed[:, :share_rows] / math.sqrt(steps_all * species)
    species_tm = summed[:, share_rows:]

    small = jnp.concatenate([time_part, species_tm], axis=1)
    small_sum = gather_blocks(small, "node").sum(0)
    grad_time = small_sum[:, :time_dev] / math.sqrt(nodes_all * species)
    grad_species = small_sum[:, time_dev:] / math.sqrt(nodes_all * steps_all)
    return (grad_node, grad_time, grad_species)


def solution(mesh):
    in_specs = (P("node", "tm"), P(None, ("node", "tm")), P(None, "tm"), P())
    out_specs = (P(None, ("node", "tm")), P(None, "tm"), P())
    return jax.shard_map(shards, mesh=mesh, in_specs=in_specs, out_specs=out_specs, check_vma=False)
```

```python
import math

import jax
import jax.numpy as jnp
from jax import lax
from jax.experimental import pallas as pl
from jax.experimental.pallas import tpu as pltpu
from jax.sharding import PartitionSpec as P

ROW_TILE = 512


def fused_kernel(obs_ref, factor_t_ref, factor_ref, khatri_ref, node_ref, contracted_ref):
    step = pl.program_id(0)
    khatri = khatri_ref[...]
    modelled = jnp.dot(factor_t_ref[...], khatri, preferred_element_type=jnp.float32)
    derivative = ((modelled - obs_ref[...].astype(jnp.float32)) / (modelled * modelled)).astype(
        jnp.bfloat16
    )
    node_ref[...] = lax.dot_general(
        khatri, derivative, (((1,), (1,)), ((), ())), preferred_element_type=jnp.float32
    )
    part = jnp.dot(factor_ref[...], derivative, preferred_element_type=jnp.float32)

    @pl.when(step == 0)
    def _():
        contracted_ref[...] = part

    @pl.when(step > 0)
    def _():
        contracted_ref[...] += part


def fused(observed, factor_t, factor, khatri):
    rows, width = observed.shape
    rank = factor.shape[0]
    tile = min(ROW_TILE, rows)
    return pl.pallas_call(
        fused_kernel,
        grid=(rows // tile,),
        in_specs=[
            pl.BlockSpec((tile, width), lambda i: (i, 0)),
            pl.BlockSpec((tile, rank), lambda i: (i, 0)),
            pl.BlockSpec((rank, tile), lambda i: (0, i)),
            pl.BlockSpec((rank, width), lambda i: (0, 0)),
        ],
        out_specs=[
            pl.BlockSpec((rank, tile), lambda i: (0, i)),
            pl.BlockSpec((rank, width), lambda i: (0, 0)),
        ],
        out_shape=[
            jax.ShapeDtypeStruct((rank, rows), jnp.float32),
            jax.ShapeDtypeStruct((rank, width), jnp.float32),
        ],
        compiler_params=pltpu.CompilerParams(dimension_semantics=("arbitrary",)),
    )(observed, factor_t, factor, khatri)


def gather_blocks(values, axis):
    count = lax.axis_size(axis)
    copies = jnp.broadcast_to(values[None], (count, *values.shape))
    return lax.all_to_all(copies, axis, 0, 0, tiled=True)


def shards(observed, node_factor, time_factor, species_factor):
    factor_rank = node_factor.shape[0]
    time_vals = time_factor.astype(jnp.float32)
    species_vals = species_factor.astype(jnp.float32)
    time_dev = time_vals.shape[1]
    species = species_vals.shape[1]
    node_rows = observed.shape[0]
    flat_width = observed.shape[1]
    tm_count = lax.axis_size("tm")
    steps_all = time_dev * tm_count
    nodes_all = node_rows * lax.axis_size("node")
    share_rows = node_rows // tm_count

    khatri = (
        (time_vals[:, :, None] * species_vals[:, None, :])
        .reshape(factor_rank, flat_width)
        .astype(jnp.bfloat16)
    )
    gathered = gather_blocks(node_factor, "tm")
    factor = gathered.transpose(1, 0, 2).reshape(factor_rank, node_rows)
    factor_t = gathered.transpose(0, 2, 1).reshape(node_rows, factor_rank)
    node_part, contracted_t = fused(observed, factor_t, factor, khatri)
    by_step = contracted_t.reshape(factor_rank, time_dev, species)
    time_part = (by_step * species_vals[:, None, :]).sum(2)
    species_part = (by_step * time_vals[:, :, None]).sum(1)

    blocks = node_part.reshape(factor_rank, tm_count, share_rows).transpose(1, 0, 2)
    riders = jnp.broadcast_to(species_part[None], (tm_count, factor_rank, species))
    payload = jnp.concatenate([blocks, riders], axis=2)
    summed = lax.all_to_all(payload, "tm", 0, 0, tiled=True).sum(0)
    grad_node = summed[:, :share_rows] / math.sqrt(steps_all * species)
    species_tm = summed[:, share_rows:]

    small = jnp.concatenate([time_part, species_tm], axis=1)
    small_sum = gather_blocks(small, "node").sum(0)
    grad_time = small_sum[:, :time_dev] / math.sqrt(nodes_all * species)
    grad_species = small_sum[:, time_dev:] / math.sqrt(nodes_all * steps_all)
    return (grad_node, grad_time, grad_species)


def solution(mesh):
    in_specs = (P("node", "tm"), P(None, ("node", "tm")), P(None, "tm"), P())
    out_specs = (P(None, ("node", "tm")), P(None, "tm"), P())
    return jax.shard_map(shards, mesh=mesh, in_specs=in_specs, out_specs=out_specs, check_vma=False)
```

```python
import math

import jax
import jax.numpy as jnp
from jax import lax
from jax.experimental import pallas as pl
from jax.experimental.pallas import tpu as pltpu
from jax.sharding import PartitionSpec as P

ROW_TILE = 512


def fused_kernel(obs_ref, factor_t_ref, factor_ref, khatri_ref, node_ref, contracted_ref):
    step = pl.program_id(0)
    khatri = khatri_ref[...]
    modelled = jnp.dot(factor_t_ref[...], khatri, preferred_element_type=jnp.float32)
    derivative = ((modelled - obs_ref[...].astype(jnp.float32)) / (modelled * modelled)).astype(
        jnp.bfloat16
    )
    node_ref[...] = lax.dot_general(
        khatri, derivative, (((1,), (1,)), ((), ())), preferred_element_type=jnp.float32
    )
    part = jnp.dot(factor_ref[...], derivative, preferred_element_type=jnp.float32)

    @pl.when(step == 0)
    def _():
        contracted_ref[...] = part

    @pl.when(step > 0)
    def _():
        contracted_ref[...] += part


def fused(observed, factor_t, factor, khatri):
    rows, width = observed.shape
    rank = factor.shape[0]
    tile = min(ROW_TILE, rows)
    return pl.pallas_call(
        fused_kernel,
        grid=(rows // tile,),
        in_specs=[
            pl.BlockSpec((tile, width), lambda i: (i, 0)),
            pl.BlockSpec((tile, rank), lambda i: (i, 0)),
            pl.BlockSpec((rank, tile), lambda i: (0, i)),
            pl.BlockSpec((rank, width), lambda i: (0, 0)),
        ],
        out_specs=[
            pl.BlockSpec((rank, tile), lambda i: (0, i)),
            pl.BlockSpec((rank, width), lambda i: (0, 0)),
        ],
        out_shape=[
            jax.ShapeDtypeStruct((rank, rows), jnp.float32),
            jax.ShapeDtypeStruct((rank, width), jnp.float32),
        ],
        compiler_params=pltpu.CompilerParams(dimension_semantics=("arbitrary",)),
    )(observed, factor_t, factor, khatri)


def gather_blocks(values, axis):
    count = lax.axis_size(axis)
    copies = jnp.broadcast_to(values[None], (count, *values.shape))
    return lax.all_to_all(copies, axis, 0, 0, tiled=True)


def butterfly_sum(values, axis):
    count = lax.axis_size(axis)
    rounds = count.bit_length() - 1
    for k in range(rounds):
        pairs = [(i, i ^ (1 << k)) for i in range(count)]
        values = values + lax.ppermute(values, axis, pairs)
    return values


def shards(observed, node_factor, time_factor, species_factor):
    factor_rank = node_factor.shape[0]
    time_vals = time_factor.astype(jnp.float32)
    species_vals = species_factor.astype(jnp.float32)
    time_dev = time_vals.shape[1]
    species = species_vals.shape[1]
    node_rows = observed.shape[0]
    flat_width = observed.shape[1]
    tm_count = lax.axis_size("tm")
    steps_all = time_dev * tm_count
    nodes_all = node_rows * lax.axis_size("node")
    share_rows = node_rows // tm_count

    khatri = (
        (time_vals[:, :, None] * species_vals[:, None, :])
        .reshape(factor_rank, flat_width)
        .astype(jnp.bfloat16)
    )
    gathered = gather_blocks(node_factor, "tm")
    factor = gathered.transpose(1, 0, 2).reshape(factor_rank, node_rows)
    factor_t = gathered.transpose(0, 2, 1).reshape(node_rows, factor_rank)
    node_part, contracted_t = fused(observed, factor_t, factor, khatri)
    by_step = contracted_t.reshape(factor_rank, time_dev, species)
    time_part = (by_step * species_vals[:, None, :]).sum(2)
    species_part = (by_step * time_vals[:, :, None]).sum(1)

    small = jnp.concatenate([time_part, species_part], axis=1)
    small_sum = butterfly_sum(small, "node")
    grad_time = small_sum[:, :time_dev] / math.sqrt(nodes_all * species)
    species_sum = butterfly_sum(small_sum[:, time_dev:], "tm")
    grad_species = species_sum / math.sqrt(nodes_all * steps_all)

    blocks = node_part.reshape(factor_rank, tm_count, share_rows).transpose(1, 0, 2)
    summed = lax.all_to_all(blocks, "tm", 0, 0, tiled=True).sum(0)
    grad_node = summed / math.sqrt(steps_all * species)
    return (grad_node, grad_time, grad_species)


def solution(mesh):
    in_specs = (P("node", "tm"), P(None, ("node", "tm")), P(None, "tm"), P())
    out_specs = (P(None, ("node", "tm")), P(None, "tm"), P())
    return jax.shard_map(shards, mesh=mesh, in_specs=in_specs, out_specs=out_specs, check_vma=False)
```

```python
import math

import jax
import jax.numpy as jnp
from jax import lax
from jax.experimental import pallas as pl
from jax.experimental.pallas import tpu as pltpu
from jax.sharding import PartitionSpec as P

ROW_TILE = 512


def fused_kernel(obs_ref, gathered_ref, khatri_ref, node_ref, contracted_ref):
    step = pl.program_id(0)
    pieces, _, piece = gathered_ref.shape
    khatri = khatri_ref[...]
    factor = jnp.concatenate([gathered_ref[c] for c in range(pieces)], axis=1)
    modelled = lax.dot_general(
        factor, khatri, (((0,), (0,)), ((), ())), preferred_element_type=jnp.float32
    )
    derivative = ((modelled - obs_ref[...].astype(jnp.float32)) / (modelled * modelled)).astype(
        jnp.bfloat16
    )
    node = lax.dot_general(
        khatri, derivative, (((1,), (1,)), ((), ())), preferred_element_type=jnp.float32
    )
    for c in range(pieces):
        node_ref[c] = node[:, c * piece : (c + 1) * piece]
    part = jnp.dot(factor, derivative, preferred_element_type=jnp.float32)

    @pl.when(step == 0)
    def _():
        contracted_ref[...] = part

    @pl.when(step > 0)
    def _():
        contracted_ref[...] += part


def fused(observed, gathered, khatri):
    rows, width = observed.shape
    count, rank, piece = gathered.shape
    tile = min(ROW_TILE, rows)
    pieces = tile // piece
    return pl.pallas_call(
        fused_kernel,
        grid=(rows // tile,),
        in_specs=[
            pl.BlockSpec((tile, width), lambda i: (i, 0)),
            pl.BlockSpec((pieces, rank, piece), lambda i: (i, 0, 0)),
            pl.BlockSpec((rank, width), lambda i: (0, 0)),
        ],
        out_specs=[
            pl.BlockSpec((pieces, rank, piece), lambda i: (i, 0, 0)),
            pl.BlockSpec((rank, width), lambda i: (0, 0)),
        ],
        out_shape=[
            jax.ShapeDtypeStruct((count, rank, piece), jnp.float32),
            jax.ShapeDtypeStruct((rank, width), jnp.float32),
        ],
        compiler_params=pltpu.CompilerParams(dimension_semantics=("arbitrary",)),
    )(observed, gathered, khatri)


def gather_blocks(values, axis):
    count = lax.axis_size(axis)
    copies = jnp.broadcast_to(values[None], (count, *values.shape))
    return lax.all_to_all(copies, axis, 0, 0, tiled=True)


def butterfly_sum(values, axis):
    count = lax.axis_size(axis)
    rounds = count.bit_length() - 1
    for k in range(rounds):
        pairs = [(i, i ^ (1 << k)) for i in range(count)]
        values = values + lax.ppermute(values, axis, pairs)
    return values


def shards(observed, node_factor, time_factor, species_factor):
    factor_rank = node_factor.shape[0]
    time_vals = time_factor.astype(jnp.float32)
    species_vals = species_factor.astype(jnp.float32)
    time_dev = time_vals.shape[1]
    species = species_vals.shape[1]
    node_rows = observed.shape[0]
    flat_width = observed.shape[1]
    tm_count = lax.axis_size("tm")
    steps_all = time_dev * tm_count
    nodes_all = node_rows * lax.axis_size("node")

    khatri = (
        (time_vals[:, :, None] * species_vals[:, None, :])
        .reshape(factor_rank, flat_width)
        .astype(jnp.bfloat16)
    )
    gathered = gather_blocks(node_factor, "tm")
    blocks, contracted_t = fused(observed, gathered, khatri)
    by_step = contracted_t.reshape(factor_rank, time_dev, species)
    time_part = (by_step * species_vals[:, None, :]).sum(2)
    species_part = (by_step * time_vals[:, :, None]).sum(1)

    small = jnp.concatenate([time_part, species_part], axis=1)
    small_sum = butterfly_sum(small, "node")
    grad_time = small_sum[:, :time_dev] / math.sqrt(nodes_all * species)
    species_sum = butterfly_sum(small_sum[:, time_dev:], "tm")
    grad_species = species_sum / math.sqrt(nodes_all * steps_all)

    summed = lax.all_to_all(blocks, "tm", 0, 0, tiled=True).sum(0)
    grad_node = summed / math.sqrt(steps_all * species)
    return (grad_node, grad_time, grad_species)


def solution(mesh):
    in_specs = (P("node", "tm"), P(None, ("node", "tm")), P(None, "tm"), P())
    out_specs = (P(None, ("node", "tm")), P(None, "tm"), P())
    return jax.shard_map(shards, mesh=mesh, in_specs=in_specs, out_specs=out_specs, check_vma=False)
```

```python
import math

import jax
import jax.numpy as jnp
from jax import lax
from jax.experimental import pallas as pl
from jax.experimental.pallas import tpu as pltpu
from jax.sharding import PartitionSpec as P

ROW_TILE = 512


def fused_kernel(obs_ref, gathered_ref, khatri_ref, node_ref, contracted_ref):
    step = pl.program_id(0)
    pieces, _, piece = gathered_ref.shape
    khatri = khatri_ref[...]
    factor = jnp.concatenate([gathered_ref[c] for c in range(pieces)], axis=1)
    modelled = lax.dot_general(
        factor, khatri, (((0,), (0,)), ((), ())), preferred_element_type=jnp.float32
    )
    derivative = ((modelled - obs_ref[...].astype(jnp.float32)) / (modelled * modelled)).astype(
        jnp.bfloat16
    )
    node = lax.dot_general(
        khatri, derivative, (((1,), (1,)), ((), ())), preferred_element_type=jnp.float32
    )
    for c in range(pieces):
        node_ref[c] = node[:, c * piece : (c + 1) * piece]
    part = lax.dot_general(
        derivative, factor, (((0,), (1,)), ((), ())), preferred_element_type=jnp.float32
    )

    @pl.when(step == 0)
    def _():
        contracted_ref[...] = part

    @pl.when(step > 0)
    def _():
        contracted_ref[...] += part


def fused(observed, gathered, khatri):
    rows, width = observed.shape
    count, rank, piece = gathered.shape
    tile = min(ROW_TILE, rows)
    pieces = tile // piece
    return pl.pallas_call(
        fused_kernel,
        grid=(rows // tile,),
        in_specs=[
            pl.BlockSpec((tile, width), lambda i: (i, 0)),
            pl.BlockSpec((pieces, rank, piece), lambda i: (i, 0, 0)),
            pl.BlockSpec((rank, width), lambda i: (0, 0)),
        ],
        out_specs=[
            pl.BlockSpec((pieces, rank, piece), lambda i: (i, 0, 0)),
            pl.BlockSpec((width, rank), lambda i: (0, 0)),
        ],
        out_shape=[
            jax.ShapeDtypeStruct((count, rank, piece), jnp.float32),
            jax.ShapeDtypeStruct((width, rank), jnp.float32),
        ],
        compiler_params=pltpu.CompilerParams(dimension_semantics=("arbitrary",)),
    )(observed, gathered, khatri)


def gather_blocks(values, axis):
    count = lax.axis_size(axis)
    copies = jnp.broadcast_to(values[None], (count, *values.shape))
    return lax.all_to_all(copies, axis, 0, 0, tiled=True)


def butterfly_sum(values, axis):
    count = lax.axis_size(axis)
    rounds = count.bit_length() - 1
    for k in range(rounds):
        pairs = [(i, i ^ (1 << k)) for i in range(count)]
        values = values + lax.ppermute(values, axis, pairs)
    return values


def shards(observed, node_factor, time_factor, species_factor):
    factor_rank = node_factor.shape[0]
    time_vals = time_factor.astype(jnp.float32)
    species_vals = species_factor.astype(jnp.float32)
    time_dev = time_vals.shape[1]
    species = species_vals.shape[1]
    node_rows = observed.shape[0]
    flat_width = observed.shape[1]
    tm_count = lax.axis_size("tm")
    steps_all = time_dev * tm_count
    nodes_all = node_rows * lax.axis_size("node")

    khatri = (
        (time_vals[:, :, None] * species_vals[:, None, :])
        .reshape(factor_rank, flat_width)
        .astype(jnp.bfloat16)
    )
    gathered = gather_blocks(node_factor, "tm")
    blocks, contracted = fused(observed, gathered, khatri)
    by_step = contracted.reshape(time_dev, species, factor_rank)
    time_part = (by_step * species_vals.T[None, :, :]).sum(1).T
    species_part = (by_step * time_vals.T[:, None, :]).sum(0).T

    small = jnp.concatenate([time_part, species_part], axis=1)
    small_sum = butterfly_sum(small, "node")
    grad_time = small_sum[:, :time_dev] / math.sqrt(nodes_all * species)
    species_sum = butterfly_sum(small_sum[:, time_dev:], "tm")
    grad_species = species_sum / math.sqrt(nodes_all * steps_all)

    summed = lax.all_to_all(blocks, "tm", 0, 0, tiled=True).sum(0)
    grad_node = summed / math.sqrt(steps_all * species)
    return (grad_node, grad_time, grad_species)


def solution(mesh):
    in_specs = (P("node", "tm"), P(None, ("node", "tm")), P(None, "tm"), P())
    out_specs = (P(None, ("node", "tm")), P(None, "tm"), P())
    return jax.shard_map(shards, mesh=mesh, in_specs=in_specs, out_specs=out_specs, check_vma=False)
```

```python
import math

import jax
import jax.numpy as jnp
from jax import lax
from jax.experimental import pallas as pl
from jax.experimental.pallas import tpu as pltpu
from jax.sharding import PartitionSpec as P

ROW_TILE = 1024


def fused_kernel(obs_ref, gathered_ref, khatri_ref, node_ref, contracted_ref):
    step = pl.program_id(0)
    pieces, _, piece = gathered_ref.shape
    khatri = khatri_ref[...]
    factor = jnp.concatenate([gathered_ref[c] for c in range(pieces)], axis=1)
    modelled = lax.dot_general(
        factor, khatri, (((0,), (0,)), ((), ())), preferred_element_type=jnp.float32
    )
    derivative = ((modelled - obs_ref[...].astype(jnp.float32)) / (modelled * modelled)).astype(
        jnp.bfloat16
    )
    node = lax.dot_general(
        derivative, khatri, (((1,), (1,)), ((), ())), preferred_element_type=jnp.float32
    ).T
    for c in range(pieces):
        node_ref[c] = node[:, c * piece : (c + 1) * piece]
    part = jnp.dot(factor, derivative, preferred_element_type=jnp.float32)

    @pl.when(step == 0)
    def _():
        contracted_ref[...] = part

    @pl.when(step > 0)
    def _():
        contracted_ref[...] += part


def fused(observed, gathered, khatri):
    rows, width = observed.shape
    count, rank, piece = gathered.shape
    tile = min(ROW_TILE, rows)
    pieces = tile // piece
    return pl.pallas_call(
        fused_kernel,
        grid=(rows // tile,),
        in_specs=[
            pl.BlockSpec((tile, width), lambda i: (i, 0)),
            pl.BlockSpec((pieces, rank, piece), lambda i: (i, 0, 0)),
            pl.BlockSpec((rank, width), lambda i: (0, 0)),
        ],
        out_specs=[
            pl.BlockSpec((pieces, rank, piece), lambda i: (i, 0, 0)),
            pl.BlockSpec((rank, width), lambda i: (0, 0)),
        ],
        out_shape=[
            jax.ShapeDtypeStruct((count, rank, piece), jnp.float32),
            jax.ShapeDtypeStruct((rank, width), jnp.float32),
        ],
        compiler_params=pltpu.CompilerParams(dimension_semantics=("arbitrary",)),
    )(observed, gathered, khatri)


def gather_blocks(values, axis):
    count = lax.axis_size(axis)
    copies = jnp.broadcast_to(values[None], (count, *values.shape))
    return lax.all_to_all(copies, axis, 0, 0, tiled=True)


def butterfly_sum(values, axis):
    count = lax.axis_size(axis)
    rounds = count.bit_length() - 1
    for k in range(rounds):
        pairs = [(i, i ^ (1 << k)) for i in range(count)]
        values = values + lax.ppermute(values, axis, pairs)
    return values


def shards(observed, node_factor, time_factor, species_factor):
    factor_rank = node_factor.shape[0]
    time_vals = time_factor.astype(jnp.float32)
    species_vals = species_factor.astype(jnp.float32)
    time_dev = time_vals.shape[1]
    species = species_vals.shape[1]
    node_rows = observed.shape[0]
    flat_width = observed.shape[1]
    tm_count = lax.axis_size("tm")
    steps_all = time_dev * tm_count
    nodes_all = node_rows * lax.axis_size("node")

    khatri = (
        (time_vals[:, :, None] * species_vals[:, None, :])
        .reshape(factor_rank, flat_width)
        .astype(jnp.bfloat16)
    )
    gathered = gather_blocks(node_factor, "tm")
    blocks, contracted_t = fused(observed, gathered, khatri)
    by_step = contracted_t.reshape(factor_rank, time_dev, species)
    time_part = (by_step * species_vals[:, None, :]).sum(2)
    species_part = (by_step * time_vals[:, :, None]).sum(1)

    small = jnp.concatenate([time_part, species_part], axis=1)
    small_sum = butterfly_sum(small, "node")
    grad_time = small_sum[:, :time_dev] / math.sqrt(nodes_all * species)
    species_sum = butterfly_sum(small_sum[:, time_dev:], "tm")
    grad_species = species_sum / math.sqrt(nodes_all * steps_all)

    summed = lax.all_to_all(blocks, "tm", 0, 0, tiled=True).sum(0)
    grad_node = summed / math.sqrt(steps_all * species)
    return (grad_node, grad_time, grad_species)


def solution(mesh):
    in_specs = (P("node", "tm"), P(None, ("node", "tm")), P(None, "tm"), P())
    out_specs = (P(None, ("node", "tm")), P(None, "tm"), P())
    return jax.shard_map(shards, mesh=mesh, in_specs=in_specs, out_specs=out_specs, check_vma=False)
```

```python
import math

import jax
import jax.numpy as jnp
from jax import lax
from jax.experimental import pallas as pl
from jax.experimental.pallas import tpu as pltpu
from jax.sharding import PartitionSpec as P

ROW_TILE = 1024


def fused_kernel(obs_ref, gathered_ref, khatri_ref, node_ref, contracted_ref):
    step = pl.program_id(0)
    pieces, _, piece = gathered_ref.shape
    khatri = khatri_ref[...]
    factor = jnp.concatenate([gathered_ref[c] for c in range(pieces)], axis=1)
    modelled = lax.dot_general(
        factor, khatri, (((0,), (0,)), ((), ())), preferred_element_type=jnp.float32
    )
    derivative = ((modelled - obs_ref[...].astype(jnp.float32)) / (modelled * modelled)).astype(
        jnp.bfloat16
    )
    node = lax.dot_general(
        derivative, khatri, (((1,), (1,)), ((), ())), preferred_element_type=jnp.float32
    ).T
    for c in range(pieces):
        node_ref[c] = node[:, c * piece : (c + 1) * piece]
    part = jnp.dot(factor, derivative, preferred_element_type=jnp.float32)

    @pl.when(step == 0)
    def _():
        contracted_ref[...] = part

    @pl.when(step > 0)
    def _():
        contracted_ref[...] += part


def fused(observed, gathered, khatri):
    rows, width = observed.shape
    count, rank, piece = gathered.shape
    tile = min(ROW_TILE, rows)
    pieces = tile // piece
    return pl.pallas_call(
        fused_kernel,
        grid=(rows // tile,),
        in_specs=[
            pl.BlockSpec((tile, width), lambda i: (i, 0)),
            pl.BlockSpec((pieces, rank, piece), lambda i: (i, 0, 0)),
            pl.BlockSpec((rank, width), lambda i: (0, 0)),
        ],
        out_specs=[
            pl.BlockSpec((pieces, rank, piece), lambda i: (i, 0, 0)),
            pl.BlockSpec((rank, width), lambda i: (0, 0)),
        ],
        out_shape=[
            jax.ShapeDtypeStruct((count, rank, piece), jnp.float32),
            jax.ShapeDtypeStruct((rank, width), jnp.float32),
        ],
        compiler_params=pltpu.CompilerParams(dimension_semantics=("arbitrary",)),
    )(observed, gathered, khatri)


def gather_blocks(values, axis):
    count = lax.axis_size(axis)
    copies = jnp.broadcast_to(values[None], (count, *values.shape))
    return lax.all_to_all(copies, axis, 0, 0, tiled=True)


def butterfly_sum(values, axis):
    count = lax.axis_size(axis)
    rounds = count.bit_length() - 1
    for k in range(rounds):
        pairs = [(i, i ^ (1 << k)) for i in range(count)]
        values = values + lax.ppermute(values, axis, pairs)
    return values


def shards(observed, node_factor, time_factor, species_factor):
    factor_rank = node_factor.shape[0]
    time_vals = time_factor.astype(jnp.float32)
    species_vals = species_factor.astype(jnp.float32)
    time_dev = time_vals.shape[1]
    species = species_vals.shape[1]
    node_rows = observed.shape[0]
    flat_width = observed.shape[1]
    tm_count = lax.axis_size("tm")
    steps_all = time_dev * tm_count
    nodes_all = node_rows * lax.axis_size("node")

    khatri = (
        (time_vals[:, :, None] * species_vals[:, None, :])
        .reshape(factor_rank, flat_width)
        .astype(jnp.bfloat16)
    )
    gathered = gather_blocks(node_factor, "tm")
    blocks, contracted_t = fused(observed, gathered, khatri)
    column = jnp.arange(flat_width)
    step_of = (column[:, None] // species == jnp.arange(time_dev)[None, :]).astype(jnp.float32)
    species_of = (column[:, None] % species == jnp.arange(species)[None, :]).astype(jnp.float32)
    species_wide = jnp.tile(species_vals, (1, time_dev))
    time_wide = jnp.repeat(time_vals, species, axis=1)
    time_part = jnp.dot(contracted_t * species_wide, step_of, precision=lax.Precision.HIGHEST)
    species_part = jnp.dot(contracted_t * time_wide, species_of, precision=lax.Precision.HIGHEST)

    small = jnp.concatenate([time_part, species_part], axis=1)
    small_sum = butterfly_sum(small, "node")
    grad_time = small_sum[:, :time_dev] / math.sqrt(nodes_all * species)
    species_sum = butterfly_sum(small_sum[:, time_dev:], "tm")
    grad_species = species_sum / math.sqrt(nodes_all * steps_all)

    summed = lax.all_to_all(blocks, "tm", 0, 0, tiled=True).sum(0)
    grad_node = summed / math.sqrt(steps_all * species)
    return (grad_node, grad_time, grad_species)


def solution(mesh):
    in_specs = (P("node", "tm"), P(None, ("node", "tm")), P(None, "tm"), P())
    out_specs = (P(None, ("node", "tm")), P(None, "tm"), P())
    return jax.shard_map(shards, mesh=mesh, in_specs=in_specs, out_specs=out_specs, check_vma=False)
```

```python
import math

import jax
import jax.numpy as jnp
from jax import lax
from jax.experimental import pallas as pl
from jax.experimental.pallas import tpu as pltpu
from jax.sharding import PartitionSpec as P

ROW_TILE = 1024


def fused_kernel(
    obs_ref, gathered_ref, khatri_ref, species_wide_ref, time_wide_ref,
    node_ref, time_ref, species_ref, contracted_ref,
):
    step = pl.program_id(0)
    pieces, _, piece = gathered_ref.shape
    khatri = khatri_ref[...]
    factor = jnp.concatenate([gathered_ref[c] for c in range(pieces)], axis=1)
    modelled = lax.dot_general(
        factor, khatri, (((0,), (0,)), ((), ())), preferred_element_type=jnp.float32
    )
    derivative = ((modelled - obs_ref[...].astype(jnp.float32)) / (modelled * modelled)).astype(
        jnp.bfloat16
    )
    node = lax.dot_general(
        derivative, khatri, (((1,), (1,)), ((), ())), preferred_element_type=jnp.float32
    ).T
    for c in range(pieces):
        node_ref[c] = node[:, c * piece : (c + 1) * piece]
    part = jnp.dot(factor, derivative, preferred_element_type=jnp.float32)

    @pl.when(step == 0)
    def _():
        contracted_ref[...] = part

    @pl.when(step > 0)
    def _():
        contracted_ref[...] += part

    @pl.when(step == pl.num_programs(0) - 1)
    def _():
        contracted = contracted_ref[...]
        width = contracted.shape[1]
        steps = time_ref.shape[1]
        kinds = species_ref.shape[1]
        column = lax.broadcasted_iota(jnp.int32, (width, steps), 0)
        step_of = (column // kinds == lax.broadcasted_iota(jnp.int32, (width, steps), 1))
        column = lax.broadcasted_iota(jnp.int32, (width, kinds), 0)
        kind_of = (column % kinds == lax.broadcasted_iota(jnp.int32, (width, kinds), 1))
        time_ref[...] = jnp.dot(
            contracted * species_wide_ref[...], step_of.astype(jnp.float32),
            precision=lax.Precision.HIGHEST, preferred_element_type=jnp.float32,
        )
        species_ref[...] = jnp.dot(
            contracted * time_wide_ref[...], kind_of.astype(jnp.float32),
            precision=lax.Precision.HIGHEST, preferred_element_type=jnp.float32,
        )


def fused(observed, gathered, khatri, species_wide, time_wide, steps, kinds):
    rows, width = observed.shape
    count, rank, piece = gathered.shape
    tile = min(ROW_TILE, rows)
    pieces = tile // piece
    return pl.pallas_call(
        fused_kernel,
        grid=(rows // tile,),
        in_specs=[
            pl.BlockSpec((tile, width), lambda i: (i, 0)),
            pl.BlockSpec((pieces, rank, piece), lambda i: (i, 0, 0)),
            pl.BlockSpec((rank, width), lambda i: (0, 0)),
            pl.BlockSpec((rank, width), lambda i: (0, 0)),
            pl.BlockSpec((rank, width), lambda i: (0, 0)),
        ],
        out_specs=[
            pl.BlockSpec((pieces, rank, piece), lambda i: (i, 0, 0)),
            pl.BlockSpec((rank, steps), lambda i: (0, 0)),
            pl.BlockSpec((rank, kinds), lambda i: (0, 0)),
        ],
        out_shape=[
            jax.ShapeDtypeStruct((count, rank, piece), jnp.float32),
            jax.ShapeDtypeStruct((rank, steps), jnp.float32),
            jax.ShapeDtypeStruct((rank, kinds), jnp.float32),
        ],
        scratch_shapes=[pltpu.VMEM((rank, width), jnp.float32)],
        compiler_params=pltpu.CompilerParams(dimension_semantics=("arbitrary",)),
    )(observed, gathered, khatri, species_wide, time_wide)


def gather_blocks(values, axis):
    count = lax.axis_size(axis)
    copies = jnp.broadcast_to(values[None], (count, *values.shape))
    return lax.all_to_all(copies, axis, 0, 0, tiled=True)


def butterfly_sum(values, axis):
    count = lax.axis_size(axis)
    rounds = count.bit_length() - 1
    for k in range(rounds):
        pairs = [(i, i ^ (1 << k)) for i in range(count)]
        values = values + lax.ppermute(values, axis, pairs)
    return values


def shards(observed, node_factor, time_factor, species_factor):
    factor_rank = node_factor.shape[0]
    time_vals = time_factor.astype(jnp.float32)
    species_vals = species_factor.astype(jnp.float32)
    time_dev = time_vals.shape[1]
    species = species_vals.shape[1]
    node_rows = observed.shape[0]
    flat_width = observed.shape[1]
    tm_count = lax.axis_size("tm")
    steps_all = time_dev * tm_count
    nodes_all = node_rows * lax.axis_size("node")

    khatri = (
        (time_vals[:, :, None] * species_vals[:, None, :])
        .reshape(factor_rank, flat_width)
        .astype(jnp.bfloat16)
    )
    gathered = gather_blocks(node_factor, "tm")
    species_wide = jnp.tile(species_vals, (1, time_dev))
    time_wide = jnp.repeat(time_vals, species, axis=1)
    blocks, time_part, species_part = fused(
        observed, gathered, khatri, species_wide, time_wide, time_dev, species
    )

    small = jnp.concatenate([time_part, species_part], axis=1)
    small_sum = butterfly_sum(small, "node")
    grad_time = small_sum[:, :time_dev] / math.sqrt(nodes_all * species)
    species_sum = butterfly_sum(small_sum[:, time_dev:], "tm")
    grad_species = species_sum / math.sqrt(nodes_all * steps_all)

    summed = lax.all_to_all(blocks, "tm", 0, 0, tiled=True).sum(0)
    grad_node = summed / math.sqrt(steps_all * species)
    return (grad_node, grad_time, grad_species)


def solution(mesh):
    in_specs = (P("node", "tm"), P(None, ("node", "tm")), P(None, "tm"), P())
    out_specs = (P(None, ("node", "tm")), P(None, "tm"), P())
    return jax.shard_map(shards, mesh=mesh, in_specs=in_specs, out_specs=out_specs, check_vma=False)
```

```python
import functools
import math

import jax
import jax.numpy as jnp
from jax import lax
from jax.experimental import pallas as pl
from jax.experimental.pallas import tpu as pltpu
from jax.sharding import PartitionSpec as P

ROW_TILE = 1024


def fused_kernel(obs_ref, gathered_ref, khatri_ref, node_ref, contracted_ref, *, node_scale):
    step = pl.program_id(0)
    pieces, _, piece = gathered_ref.shape
    khatri = khatri_ref[...]
    factor = jnp.concatenate([gathered_ref[c] for c in range(pieces)], axis=1)
    modelled = lax.dot_general(
        factor, khatri, (((0,), (0,)), ((), ())), preferred_element_type=jnp.float32
    )
    derivative = ((modelled - obs_ref[...].astype(jnp.float32)) / (modelled * modelled)).astype(
        jnp.bfloat16
    )
    node = lax.dot_general(
        derivative, khatri, (((1,), (1,)), ((), ())), preferred_element_type=jnp.float32
    ).T * node_scale
    for c in range(pieces):
        node_ref[c] = node[:, c * piece : (c + 1) * piece]
    part = jnp.dot(factor, derivative, preferred_element_type=jnp.float32)

    @pl.when(step == 0)
    def _():
        contracted_ref[...] = part

    @pl.when(step > 0)
    def _():
        contracted_ref[...] += part


def fused(observed, gathered, khatri, node_scale):
    rows, width = observed.shape
    count, rank, piece = gathered.shape
    tile = min(ROW_TILE, rows)
    pieces = tile // piece
    return pl.pallas_call(
        functools.partial(fused_kernel, node_scale=node_scale),
        grid=(rows // tile,),
        in_specs=[
            pl.BlockSpec((tile, width), lambda i: (i, 0)),
            pl.BlockSpec((pieces, rank, piece), lambda i: (i, 0, 0)),
            pl.BlockSpec((rank, width), lambda i: (0, 0)),
        ],
        out_specs=[
            pl.BlockSpec((pieces, rank, piece), lambda i: (i, 0, 0)),
            pl.BlockSpec((rank, width), lambda i: (0, 0)),
        ],
        out_shape=[
            jax.ShapeDtypeStruct((count, rank, piece), jnp.float32),
            jax.ShapeDtypeStruct((rank, width), jnp.float32),
        ],
        compiler_params=pltpu.CompilerParams(dimension_semantics=("arbitrary",)),
    )(observed, gathered, khatri)


def gather_blocks(values, axis):
    count = lax.axis_size(axis)
    copies = jnp.broadcast_to(values[None], (count, *values.shape))
    return lax.all_to_all(copies, axis, 0, 0, tiled=True)


def butterfly_sum(values, axis):
    count = lax.axis_size(axis)
    rounds = count.bit_length() - 1
    for k in range(rounds):
        pairs = [(i, i ^ (1 << k)) for i in range(count)]
        values = values + lax.ppermute(values, axis, pairs)
    return values


def exact_scale(count):
    root = math.sqrt(count)
    return 1.0 / root if root == 2.0 ** round(math.log2(root)) else None


def shards(observed, node_factor, time_factor, species_factor):
    factor_rank = node_factor.shape[0]
    time_vals = time_factor.astype(jnp.float32)
    species_vals = species_factor.astype(jnp.float32)
    time_dev = time_vals.shape[1]
    species = species_vals.shape[1]
    node_rows = observed.shape[0]
    flat_width = observed.shape[1]
    tm_count = lax.axis_size("tm")
    steps_all = time_dev * tm_count
    nodes_all = node_rows * lax.axis_size("node")

    khatri = (
        (time_vals[:, :, None] * species_vals[:, None, :])
        .reshape(factor_rank, flat_width)
        .astype(jnp.bfloat16)
    )
    node_scale = exact_scale(steps_all * species)
    time_scale = exact_scale(nodes_all * species)
    species_scale = exact_scale(nodes_all * steps_all)
    folded = None not in (node_scale, time_scale, species_scale)

    gathered = gather_blocks(node_factor, "tm")
    blocks, contracted_t = fused(observed, gathered, khatri, node_scale if folded else 1.0)
    by_step = contracted_t.reshape(factor_rank, time_dev, species)
    time_part = (by_step * species_vals[:, None, :]).sum(2)
    species_part = (by_step * time_vals[:, :, None]).sum(1)
    if folded:
        time_part = time_part * time_scale
        species_part = species_part * species_scale

    small = jnp.concatenate([time_part, species_part], axis=1)
    small_sum = butterfly_sum(small, "node")
    grad_time = small_sum[:, :time_dev]
    grad_species = butterfly_sum(small_sum[:, time_dev:], "tm")
    grad_node = lax.all_to_all(blocks, "tm", 0, 0, tiled=True).sum(0)
    if not folded:
        grad_time = grad_time / math.sqrt(nodes_all * species)
        grad_species = grad_species / math.sqrt(nodes_all * steps_all)
        grad_node = grad_node / math.sqrt(steps_all * species)
    return (grad_node, grad_time, grad_species)


def solution(mesh):
    in_specs = (P("node", "tm"), P(None, ("node", "tm")), P(None, "tm"), P())
    out_specs = (P(None, ("node", "tm")), P(None, "tm"), P())
    return jax.shard_map(shards, mesh=mesh, in_specs=in_specs, out_specs=out_specs, check_vma=False)
```
